512 devices in a mesh: rep: 4 (over y), exp: 128 (over x, z, core).
Axes of the slice: x: 4, y: 4, z: 16, core: 2. Of those that a mesh axis runs over, the one named last changes fastest.
Arguments:
- tokens: bfloat16 [16384, 2880], P('exp'), may hold values from -6 to 6
- expert_ids: int32 [16384, 4], P('exp'), may hold values from 0 to 63, all different within a row; in each aligned block of 128 rows (0 to 127, 128 to 255, ...) at most 12 rows name the same one
- gate_levels: int32 [16384, 4], P('exp'), may hold values from 1 to 255
- w_gate: bfloat16 [128, 768, 2880], P('exp', 'rep'), may hold values from -0.109375 to 0.109375
- w_up: bfloat16 [128, 768, 2880], P('exp', 'rep'), may hold values from -0.109375 to 0.109375
- w_down: bfloat16 [128, 1536, 1440], P('exp', None, 'rep'), may hold values from -0.15625 to 0.15625
Outputs:
- moe_out: bfloat16 [16384, 2, 1440], P('exp', None, 'rep')
The draws below stay inside these ranges and needn't reach their ends.
Inputs may be any that keep to these rules, and one draw needn't show every extreme that they name: `expert_ids`: each row names 4 different experts. Within the rows of one device (aligned blocks of 128 tokens) no expert is named by more than 12 rows, a bound that some block reaches.
All inputs are finite; a program needn't handle non-finite values.
Results may differ from the reference program's by a relative error of at most 0.0057.
Values may be sent and summed in bfloat16 or wider, within the bound.
No kernel may reach another device: no remote copies, remote signals or barrier semaphores. Data moves between devices by JAX's collectives and lax.ppermute only.
A program may use at most 128 MiB of HBM per device.

```python
import math
import jax
import jax.numpy as jnp
import numpy as np
from jax import lax

D = 2880
FF = 1536
TOPK = 4
TOK_DEV = 128
EXPERTS = 64
CAP = 12
TOKENS = 16384
N_EXP = 128


def set_ends(entries, own_key, low, top_value):
    extent = entries.shape
    index_at = [jax.random.randint(jax.random.fold_in(own_key, axis), (), 0, extent[axis]) for axis in range(len(extent))]
    entries = entries.at[tuple(index_at)].set(low)
    longest = extent.index(max(extent))
    index_at[longest] = (index_at[longest] + 1) % extent[longest]
    return entries.at[tuple(index_at)].set(top_value)


def block_scale(rng, extent, split, smallest, largest):
    gain, own = 1.0, jax.random.fold_in(rng, 6)
    for axis_at, shards_of in split:
        draws = jnp.exp(jax.random.uniform(jax.random.fold_in(own, axis_at), (shards_of,), jnp.float32, smallest / len(split), largest / len(split)))
        gain = gain * jnp.repeat(draws, extent[axis_at] // shards_of).reshape([-1 if axis == axis_at else 1 for axis in range(len(extent))])
    return gain


def assign_block(stream_key, own, number, rows, number_of, top, limit, lean):
    sequence = jax.random.permutation(stream_key, number_of)
    packed, ordinary = portions_of(number_of, rows * top, limit, lean, True), portions_of(number_of, rows * top, limit, lean, False)
    places = jnp.arange(number_of)

    def named(lengths, turn):
        used = int((lengths > 0).sum())
        fixed = max(1, used // 4)
        passed = fixed + (places - fixed + turn * (used - fixed)) % max(1, number_of - fixed)
        return jnp.zeros((number_of,), jnp.int32).at[sequence[jnp.where(places < fixed, places, passed)]].set(jnp.asarray(lengths, jnp.int32))

    lengths = jnp.where(number % 4 == 0, named(packed, number // 4), named(ordinary, number - number // 4 - 1))
    mixed = jax.random.permutation(jax.random.fold_in(own, 3), number_of)
    donor, sink = mixed[0:number_of // 2 * 2:2], mixed[1:number_of // 2 * 2:2]
    room = jnp.minimum(lengths[donor] - 1, limit - lengths[sink]) // 2
    room = jnp.where((donor == sequence[0]) | (sink == sequence[0]) | (lengths[sink] == 0), 0, jnp.maximum(room, 0))
    passed = jax.random.randint(jax.random.fold_in(own, 4), (number_of // 2,), 0, 1 << 20) % (room + 1)
    lengths = lengths.at[donor].add(-passed).at[sink].add(passed)
    members = jnp.searchsorted(jnp.cumsum(lengths), jnp.arange(rows * top), side="right").astype(jnp.int32)
    grid = members.reshape(top, rows).T
    grid = grid[jax.random.permutation(jax.random.fold_in(own, 1), rows)]
    turn = jax.random.randint(jax.random.fold_in(own, 2), (rows, 1), 0, top)
    return jnp.take_along_axis(grid, (jnp.arange(top)[None, :] + turn) % top, axis=1)


def portions_of(number_of, total, limit, lean, full):
    portions = [(1 << 20) // math.isqrt(grade ** lean) + 1 for grade in range(1, number_of + 1)]
    largest = limit if full else min(limit, max(-(-total // number_of), total * portions[0] // sum(portions)))
    least = 1 if total - largest >= number_of - 1 else 0
    counts, spare = [largest] + [least] * (number_of - 1), total - largest - least * (number_of - 1)
    while spare > 0:
        movable = [i for i in range(1, number_of) if counts[i] < largest] or [i for i in range(1, number_of) if counts[i] < limit]
        whole, remaining = sum([portions[i] for i in movable]), spare
        for i in movable:
            extra = min(limit - counts[i], max(1, remaining * portions[i] // whole), spare)
            counts[i] = counts[i] + extra
            spare = spare - extra
    return np.array(counts)


def centred(rng, extent, spread, bound, shards=(), held_as=jnp.bfloat16):
    values = jax.random.normal(rng, extent, jnp.float32) * spread
    if len(shards) > 0:
        values = block_scale(rng, extent, shards, -0.22, 0.18) * values
    return jnp.clip(values, min=-bound, max=bound).astype(held_as)


def setup_inputs(seed: int = 0) -> dict:
    seeds = jax.random.split(jax.random.key(seed), 7)
    tokens = centred(seeds[0], (TOKENS, D), 1.0, 6.0, ((0, 128),))
    expert_ids_keys = jax.random.split(jax.random.fold_in(seeds[1], 1), TOKENS // TOK_DEV)
    expert_ids_turns = jax.random.permutation(jax.random.fold_in(seeds[1], 3), TOKENS // TOK_DEV)
    expert_ids = jax.vmap(lambda own, number: assign_block(jax.random.fold_in(seeds[1], 2), own, number, TOK_DEV, EXPERTS, TOPK, CAP, 1))(expert_ids_keys, expert_ids_turns).reshape((TOKENS, TOPK))
    gate_levels = set_ends(jax.random.randint(seeds[2], (TOKENS, TOPK), 1, 256), jax.random.fold_in(seeds[2], 1), 1, 255).astype(jnp.int32)
    w_gate = centred(seeds[3], (EXPERTS * 2, FF // 2, D), D ** -0.5, 0.109375, ((0, 128), (1, 4)))
    w_up = centred(seeds[4], (EXPERTS * 2, FF // 2, D), D ** -0.5, 0.109375, ((0, 128), (1, 4)))
    w_down = centred(seeds[5], (EXPERTS * 2, FF, D // 2), FF ** -0.5, 0.15625, ((0, 128), (2, 4)))
    return dict(tokens=tokens, expert_ids=expert_ids, gate_levels=gate_levels, w_gate=w_gate, w_up=w_up, w_down=w_down)


def expert_apply(token_rows, gate_matrix, up_matrix, down_matrix):
    gate_proj = jnp.dot(token_rows, gate_matrix, preferred_element_type=jnp.float32)
    up_proj = jnp.dot(token_rows, up_matrix, preferred_element_type=jnp.float32)
    hidden = ((up_proj + 1.0) * gate_proj * jax.nn.sigmoid(1.702 * gate_proj)).astype(jnp.bfloat16)
    return jnp.dot(hidden, down_matrix, preferred_element_type=jnp.float32).astype(jnp.bfloat16)


def reference(tokens, expert_ids, gate_levels, w_gate, w_up, w_down):
    flat_ids = expert_ids.reshape(N_EXP, TOK_DEV * TOPK)
    onehot = (flat_ids[:, :, None] == jnp.arange(EXPERTS, dtype=jnp.int32)[None, None, :]).astype(jnp.int32)
    rank_counts = jnp.cumsum(onehot, axis=1) - onehot
    slot_index = jnp.sum(rank_counts * onehot, axis=2).astype(jnp.int32)
    block_index = jnp.arange(N_EXP, dtype=jnp.int32)[:, None]
    position = (block_index * CAP + slot_index).astype(jnp.int32)
    token_index = (block_index * TOK_DEV + jnp.arange(TOK_DEV * TOPK, dtype=jnp.int32)[None, :] // TOPK).astype(jnp.int32)
    table = jnp.full((EXPERTS, N_EXP * CAP), TOKENS, dtype=jnp.int32).at[flat_ids, position].set(token_index)
    padded = jnp.concatenate([tokens, jnp.zeros((1, D), tokens.dtype)], axis=0)
    gate_pairs = w_gate.reshape(EXPERTS, 2, FF // 2, D)
    up_pairs = w_up.reshape(EXPERTS, 2, FF // 2, D)
    down_pairs = w_down.reshape(EXPERTS, 2, FF, D // 2)

    def one_expert(expert):
        token_rows = padded[table[expert]]
        gate_pair = gate_pairs[expert]
        up_pair = up_pairs[expert]
        down_pair = down_pairs[expert]
        gate_matrix = jnp.concatenate([gate_pair[0], gate_pair[1]], axis=0).T
        up_matrix = jnp.concatenate([up_pair[0], up_pair[1]], axis=0).T
        down_matrix = jnp.concatenate([down_pair[0], down_pair[1]], axis=1)
        return expert_apply(token_rows, gate_matrix, up_matrix, down_matrix)

    results = lax.map(one_expert, jnp.arange(EXPERTS, dtype=jnp.int32))
    picked = results[flat_ids, position].astype(jnp.float32)
    levels = gate_levels.astype(jnp.float32)
    mixing = (levels / jnp.sum(levels, axis=1, keepdims=True)).reshape(N_EXP, TOK_DEV * TOPK, 1)
    weighted = (mixing * picked).reshape(TOKENS, TOPK, D)
    combined = jnp.sum(weighted, axis=1)
    return combined.astype(jnp.bfloat16).reshape(TOKENS, 2, D // 2)
```

```python
import jax
import jax.numpy as jnp
from jax import lax
from jax.sharding import Mesh
from jax.sharding import PartitionSpec as P

GROUP = "grp"
CORE = "core"
REP = "rep"


def on_device(tokens, expert_ids, gate_levels, w_gate, w_up, w_down):
    tok_rows = tokens.shape[0]
    model_width = tokens.shape[1]
    top_count = expert_ids.shape[1]
    n_rep = lax.axis_size(REP)
    expert_count = lax.axis_size(GROUP)
    capacity = min(
        tok_rows, max(4, (tok_rows * top_count * 3 // (2 * expert_count) + 3) // 4 * 4)
    )
    part = capacity // n_rep
    rep_index = lax.axis_index(REP)
    core_index = lax.axis_index(CORE)

    flat_ids = expert_ids.reshape(-1)
    onehot = (flat_ids[:, None] == jnp.arange(expert_count, dtype=jnp.int32)[None, :]).astype(
        jnp.int32
    )
    rank_counts = jnp.cumsum(onehot, axis=0) - onehot
    slot_index = jnp.sum(rank_counts * onehot, axis=1)
    source_rows = jnp.arange(tok_rows * top_count, dtype=jnp.int32) // top_count

    local_slot = slot_index - part * rep_index
    in_part = (local_slot >= 0) & (local_slot < part)
    send_slots = expert_count * part
    position = jnp.where(in_part, flat_ids * part + local_slot, send_slots)
    table = jnp.zeros((send_slots,), jnp.int32).at[position].set(source_rows, mode="drop")
    outgoing = tokens[table].reshape(expert_count, part, model_width)

    swap = [(0, 1), (1, 0)]
    other_gate, other_up, other_down = lax.ppermute((w_gate[0], w_up[0], w_down[0]), CORE, swap)

    arrived = lax.all_to_all(outgoing, GROUP, 0, 0, tiled=True)
    rows = lax.all_gather(arrived, REP, axis=0, tiled=False)
    rows = rows.reshape(-1, model_width)

    gate_units = jnp.concatenate([w_gate[0], other_gate], axis=0)
    up_units = jnp.concatenate([w_up[0], other_up], axis=0)
    contract = (((1,), (1,)), ((), ()))
    gate_proj = lax.dot_general(rows, gate_units, contract, preferred_element_type=jnp.float32)
    up_proj = lax.dot_general(rows, up_units, contract, preferred_element_type=jnp.float32)
    hidden = ((up_proj + 1.0) * gate_proj * jax.nn.sigmoid(1.702 * gate_proj)).astype(jnp.bfloat16)
    n_rows = rows.shape[0]
    quarter = w_gate.shape[1]
    hidden = hidden.reshape(n_rows, 2, quarter)
    hidden_all = lax.all_gather(hidden, REP, axis=0, tiled=False)

    down_cols = jnp.concatenate([w_down[0], other_down], axis=1)
    col_count = down_cols.shape[1]
    down_split = down_cols.reshape(2, n_rep, quarter, col_count)
    own_half = lax.dynamic_index_in_dim(down_split, core_index, 0, keepdims=False)
    other_half = lax.dynamic_index_in_dim(down_split, 1 - core_index, 0, keepdims=False)
    down_units = jnp.stack([own_half, other_half], axis=1)
    projected = jnp.einsum(
        "rnhk,rhkc->nc", hidden_all, down_units, preferred_element_type=jnp.float32
    )
    expert_out = projected.astype(jnp.bfloat16).reshape(n_rep, expert_count, part, col_count)

    returned = lax.all_to_all(expert_out, GROUP, 1, 1, tiled=True)
    returned = returned.reshape(-1, col_count)
    pick = ((slot_index // part) * expert_count + flat_ids) * part + slot_index % part
    picked = returned[pick].astype(jnp.float32)
    levels = gate_levels.astype(jnp.float32)
    mixing = (levels / jnp.sum(levels, axis=1, keepdims=True)).reshape(-1, 1)
    combined = jnp.sum((mixing * picked).reshape(tok_rows, top_count, col_count), axis=1)
    combined = combined.reshape(tok_rows, 2, col_count // 2)
    ordered = jnp.where(core_index == 0, combined, combined[:, ::-1, :])
    return ordered.astype(jnp.bfloat16)


def solution(mesh):
    n_rep = mesh.shape[REP]
    n_exp = mesh.shape["exp"]
    split = Mesh(mesh.devices.reshape(n_rep, n_exp // 2, 2), (REP, GROUP, CORE))
    shards = (GROUP, CORE)
    return jax.shard_map(
        on_device,
        mesh=split,
        in_specs=(
            P(shards, None),
            P(shards, None),
            P(shards, None),
            P(shards, REP, None),
            P(shards, REP, None),
            P(shards, None, REP),
        ),
        out_specs=P(shards, None, REP),
        check_vma=False,
    )
```

```python
import jax
import jax.numpy as jnp
from jax import lax
from jax.sharding import Mesh
from jax.sharding import PartitionSpec as P

GROUP = "grp"
CORE = "core"
REP = "rep"


def on_device(tokens, expert_ids, gate_levels, w_gate, w_up, w_down):
    tok_rows = tokens.shape[0]
    model_width = tokens.shape[1]
    top_count = expert_ids.shape[1]
    n_rep = lax.axis_size(REP)
    expert_count = lax.axis_size(GROUP)
    capacity = min(
        tok_rows, max(4, (tok_rows * top_count * 3 // (2 * expert_count) + 3) // 4 * 4)
    )
    part = capacity // n_rep
    rep_index = lax.axis_index(REP)
    core_index = lax.axis_index(CORE)

    flat_ids = expert_ids.reshape(-1)
    onehot = (flat_ids[:, None] == jnp.arange(expert_count, dtype=jnp.int32)[None, :]).astype(
        jnp.int32
    )
    rank_counts = jnp.cumsum(onehot, axis=0) - onehot
    slot_index = jnp.sum(rank_counts * onehot, axis=1)
    source_rows = jnp.arange(tok_rows * top_count, dtype=jnp.int32) // top_count

    local_slot = slot_index - part * rep_index
    in_part = (local_slot >= 0) & (local_slot < part)
    send_slots = expert_count * part
    position = jnp.where(in_part, local_slot * expert_count + flat_ids, send_slots)
    table = jnp.zeros((send_slots,), jnp.int32).at[position].set(source_rows, mode="drop")
    outgoing = tokens[table].reshape(part, expert_count, model_width)

    swap = [(0, 1), (1, 0)]
    other_gate, other_up, other_down = lax.ppermute((w_gate[0], w_up[0], w_down[0]), CORE, swap)

    arrived = lax.all_to_all(outgoing, GROUP, 1, 1, tiled=True)
    rows = lax.all_gather(arrived, REP, axis=0, tiled=False)
    rows = rows.reshape(-1, model_width)

    gate_units = jnp.concatenate([w_gate[0], other_gate], axis=0)
    up_units = jnp.concatenate([w_up[0], other_up], axis=0)
    contract = (((1,), (1,)), ((), ()))
    gate_proj = lax.dot_general(rows, gate_units, contract, preferred_element_type=jnp.float32)
    up_proj = lax.dot_general(rows, up_units, contract, preferred_element_type=jnp.float32)
    hidden = ((up_proj + 1.0) * gate_proj * jax.nn.sigmoid(1.702 * gate_proj)).astype(jnp.bfloat16)
    quarter = w_gate.shape[1]
    hidden_all = lax.all_gather(hidden, REP, axis=0, tiled=False)

    down_cols = jnp.concatenate([w_down[0], other_down], axis=1)
    col_count = down_cols.shape[1]
    down_split = down_cols.reshape(2, n_rep, quarter, col_count)
    own_half = lax.dynamic_index_in_dim(down_split, core_index, 0, keepdims=False)
    other_half = lax.dynamic_index_in_dim(down_split, 1 - core_index, 0, keepdims=False)
    down_units = jnp.stack([own_half, other_half], axis=1).reshape(n_rep, 2 * quarter, col_count)
    projected = jnp.einsum(
        "rnk,rkc->nc", hidden_all, down_units, preferred_element_type=jnp.float32
    )
    expert_out = projected.astype(jnp.bfloat16).reshape(capacity, expert_count, col_count)

    returned = lax.all_to_all(expert_out, GROUP, 1, 1, tiled=True)
    returned = returned.reshape(-1, col_count)
    pick = slot_index * expert_count + flat_ids
    picked = returned[pick].astype(jnp.float32)
    levels = gate_levels.astype(jnp.float32)
    mixing = (levels / jnp.sum(levels, axis=1, keepdims=True)).reshape(-1, 1)
    combined = jnp.sum((mixing * picked).reshape(tok_rows, top_count, col_count), axis=1)
    combined = combined.reshape(tok_rows, 2, col_count // 2)
    ordered = jnp.where(core_index == 0, combined, combined[:, ::-1, :])
    return ordered.astype(jnp.bfloat16)


def solution(mesh):
    n_rep = mesh.shape[REP]
    n_exp = mesh.shape["exp"]
    split = Mesh(mesh.devices.reshape(n_rep, n_exp // 2, 2), (REP, GROUP, CORE))
    shards = (GROUP, CORE)
    return jax.shard_map(
        on_device,
        mesh=split,
        in_specs=(
            P(shards, None),
            P(shards, None),
            P(shards, None),
            P(shards, REP, None),
            P(shards, REP, None),
            P(shards, None, REP),
        ),
        out_specs=P(shards, None, REP),
        check_vma=False,
    )
```

```python
import jax
import jax.numpy as jnp
from jax import lax
from jax.sharding import Mesh
from jax.sharding import PartitionSpec as P

GROUP = "grp"
CORE = "core"
REP = "rep"


def on_device(tokens, expert_ids, gate_levels, w_gate, w_up, w_down):
    tok_rows = tokens.shape[0]
    model_width = tokens.shape[1]
    top_count = expert_ids.shape[1]
    n_rep = lax.axis_size(REP)
    expert_count = lax.axis_size(GROUP)
    capacity = min(
        tok_rows, max(4, (tok_rows * top_count * 3 // (2 * expert_count) + 3) // 4 * 4)
    )
    part = capacity // n_rep
    rep_index = lax.axis_index(REP)
    core_index = lax.axis_index(CORE)

    flat_ids = expert_ids.reshape(-1)
    onehot = (flat_ids[:, None] == jnp.arange(expert_count, dtype=jnp.int32)[None, :]).astype(
        jnp.int32
    )
    rank_counts = jnp.cumsum(onehot, axis=0) - onehot
    slot_index = jnp.sum(rank_counts * onehot, axis=1)
    source_rows = jnp.arange(tok_rows * top_count, dtype=jnp.int32) // top_count

    local_slot = slot_index - part * rep_index
    in_part = (local_slot >= 0) & (local_slot < part)
    send_slots = expert_count * part
    position = jnp.where(in_part, local_slot * expert_count + flat_ids, send_slots)
    table = jnp.zeros((send_slots,), jnp.int32).at[position].set(source_rows, mode="drop")
    outgoing = tokens[table].reshape(part, expert_count, 1, model_width)

    swap = [(0, 1), (1, 0)]
    other_gate, other_up, other_down = lax.ppermute((w_gate[0], w_up[0], w_down[0]), CORE, swap)
    gate_units = jnp.concatenate([w_gate[0], other_gate], axis=0)
    up_units = jnp.concatenate([w_up[0], other_up], axis=0)
    quarter = w_gate.shape[1]
    down_cols = jnp.concatenate([w_down[0], other_down], axis=1)
    col_count = down_cols.shape[1]
    down_split = down_cols.reshape(2, n_rep, quarter, col_count)
    own_half = lax.dynamic_index_in_dim(down_split, core_index, 0, keepdims=False)
    other_half = lax.dynamic_index_in_dim(down_split, 1 - core_index, 0, keepdims=False)
    down_units = jnp.stack([own_half, other_half], axis=1).reshape(n_rep, 2 * quarter, col_count)
    contract = (((1,), (1,)), ((), ()))

    chunks = []
    for chunk in range(part):
        arrived = lax.all_to_all(outgoing[chunk], GROUP, 0, 0, tiled=True)
        rows = lax.all_gather(arrived, REP, axis=0, tiled=False).reshape(-1, model_width)
        gate_proj = lax.dot_general(rows, gate_units, contract, preferred_element_type=jnp.float32)
        up_proj = lax.dot_general(rows, up_units, contract, preferred_element_type=jnp.float32)
        hidden = ((up_proj + 1.0) * gate_proj * jax.nn.sigmoid(1.702 * gate_proj)).astype(
            jnp.bfloat16
        )
        hidden_all = lax.all_gather(hidden, REP, axis=0, tiled=False)
        projected = jnp.einsum(
            "rnk,rkc->nc", hidden_all, down_units, preferred_element_type=jnp.float32
        )
        expert_out = projected.astype(jnp.bfloat16).reshape(n_rep, expert_count, col_count)
        chunks.append(lax.all_to_all(expert_out, GROUP, 1, 1, tiled=True))

    returned = jnp.stack(chunks, axis=0).reshape(-1, col_count)
    pick = ((slot_index % part) * n_rep + slot_index // part) * expert_count + flat_ids
    picked = returned[pick].astype(jnp.float32)
    levels = gate_levels.astype(jnp.float32)
    mixing = (levels / jnp.sum(levels, axis=1, keepdims=True)).reshape(-1, 1)
    combined = jnp.sum((mixing * picked).reshape(tok_rows, top_count, col_count), axis=1)
    combined = combined.reshape(tok_rows, 2, col_count // 2)
    ordered = jnp.where(core_index == 0, combined, combined[:, ::-1, :])
    return ordered.astype(jnp.bfloat16)


def solution(mesh):
    n_rep = mesh.shape[REP]
    n_exp = mesh.shape["exp"]
    split = Mesh(mesh.devices.reshape(n_rep, n_exp // 2, 2), (REP, GROUP, CORE))
    shards = (GROUP, CORE)
    return jax.shard_map(
        on_device,
        mesh=split,
        in_specs=(
            P(shards, None),
            P(shards, None),
            P(shards, None),
            P(shards, REP, None),
            P(shards, REP, None),
            P(shards, None, REP),
        ),
        out_specs=P(shards, None, REP),
        check_vma=False,
    )
```

```python
import jax
import jax.numpy as jnp
from jax import lax
from jax.sharding import Mesh
from jax.sharding import PartitionSpec as P

GROUP = "grp"
CORE = "core"
REP = "rep"


def rep_shifts(value, n_rep):
    pieces = [value]
    for shift in range(1, n_rep):
        pairs = [(source, (source + shift) % n_rep) for source in range(n_rep)]
        pieces.append(lax.ppermute(value, REP, pairs))
    return jnp.stack(pieces, axis=0)


def on_device(tokens, expert_ids, gate_levels, w_gate, w_up, w_down):
    tok_rows = tokens.shape[0]
    model_width = tokens.shape[1]
    top_count = expert_ids.shape[1]
    n_rep = lax.axis_size(REP)
    expert_count = lax.axis_size(GROUP)
    capacity = min(
        tok_rows, max(4, (tok_rows * top_count * 3 // (2 * expert_count) + 3) // 4 * 4)
    )
    part = capacity // n_rep
    rep_index = lax.axis_index(REP)
    core_index = lax.axis_index(CORE)

    flat_ids = expert_ids.reshape(-1)
    onehot = (flat_ids[:, None] == jnp.arange(expert_count, dtype=jnp.int32)[None, :]).astype(
        jnp.int32
    )
    rank_counts = jnp.cumsum(onehot, axis=0) - onehot
    slot_index = jnp.sum(rank_counts * onehot, axis=1)
    source_rows = jnp.arange(tok_rows * top_count, dtype=jnp.int32) // top_count

    local_slot = slot_index - part * rep_index
    in_part = (local_slot >= 0) & (local_slot < part)
    send_slots = expert_count * part
    position = jnp.where(in_part, local_slot * expert_count + flat_ids, send_slots)
    table = jnp.zeros((send_slots,), jnp.int32).at[position].set(source_rows, mode="drop")
    outgoing = tokens[table].reshape(part, expert_count, 1, model_width)

    swap = [(0, 1), (1, 0)]
    other_gate, other_up, other_down = lax.ppermute((w_gate[0], w_up[0], w_down[0]), CORE, swap)
    gate_units = jnp.concatenate([w_gate[0], other_gate], axis=0)
    up_units = jnp.concatenate([w_up[0], other_up], axis=0)
    quarter = w_gate.shape[1]
    down_cols = jnp.concatenate([w_down[0], other_down], axis=1)
    col_count = down_cols.shape[1]
    down_split = down_cols.reshape(2, n_rep, quarter, col_count)
    own_half = lax.dynamic_index_in_dim(down_split, core_index, 0, keepdims=False)
    other_half = lax.dynamic_index_in_dim(down_split, 1 - core_index, 0, keepdims=False)
    down_units = jnp.stack([own_half, other_half], axis=1).reshape(n_rep, 2 * quarter, col_count)
    shift_source = (rep_index - jnp.arange(n_rep, dtype=jnp.int32)) % n_rep
    down_units = jnp.take(down_units, shift_source, axis=0)
    contract = (((1,), (1,)), ((), ()))

    chunks = []
    for chunk in range(part):
        arrived = lax.all_to_all(outgoing[chunk], GROUP, 0, 0, tiled=True)
        rows = jnp.take(rep_shifts(arrived, n_rep), shift_source, axis=0)
        rows = rows.reshape(-1, model_width)
        gate_proj = lax.dot_general(rows, gate_units, contract, preferred_element_type=jnp.float32)
        up_proj = lax.dot_general(rows, up_units, contract, preferred_element_type=jnp.float32)
        hidden = ((up_proj + 1.0) * gate_proj * jax.nn.sigmoid(1.702 * gate_proj)).astype(
            jnp.bfloat16
        )
        hidden_all = rep_shifts(hidden, n_rep)
        projected = jnp.einsum(
            "rnk,rkc->nc", hidden_all, down_units, preferred_element_type=jnp.float32
        )
        expert_out = projected.astype(jnp.bfloat16).reshape(n_rep, expert_count, col_count)
        chunks.append(lax.all_to_all(expert_out, GROUP, 1, 1, tiled=True))

    returned = jnp.stack(chunks, axis=0).reshape(-1, col_count)
    pick = ((slot_index % part) * n_rep + slot_index // part) * expert_count + flat_ids
    picked = returned[pick].astype(jnp.float32)
    levels = gate_levels.astype(jnp.float32)
    mixing = (levels / jnp.sum(levels, axis=1, keepdims=True)).reshape(-1, 1)
    combined = jnp.sum((mixing * picked).reshape(tok_rows, top_count, col_count), axis=1)
    combined = combined.reshape(tok_rows, 2, col_count // 2)
    ordered = jnp.where(core_index == 0, combined, combined[:, ::-1, :])
    return ordered.astype(jnp.bfloat16)


def solution(mesh):
    n_rep = mesh.shape[REP]
    n_exp = mesh.shape["exp"]
    split = Mesh(mesh.devices.reshape(n_rep, n_exp // 2, 2), (REP, GROUP, CORE))
    shards = (GROUP, CORE)
    return jax.shard_map(
        on_device,
        mesh=split,
        in_specs=(
            P(shards, None),
            P(shards, None),
            P(shards, None),
            P(shards, REP, None),
            P(shards, REP, None),
            P(shards, None, REP),
        ),
        out_specs=P(shards, None, REP),
        check_vma=False,
    )
```

```python
import jax
import jax.numpy as jnp
from jax import lax
from jax.sharding import Mesh
from jax.sharding import PartitionSpec as P

GROUP = "grp"
CORE = "core"
REP = "rep"


def on_device(tokens, expert_ids, gate_levels, w_gate, w_up, w_down):
    tok_rows = tokens.shape[0]
    model_width = tokens.shape[1]
    top_count = expert_ids.shape[1]
    n_rep = lax.axis_size(REP)
    expert_count = lax.axis_size(GROUP)
    capacity = min(
        tok_rows, max(4, (tok_rows * top_count * 3 // (2 * expert_count) + 3) // 4 * 4)
    )
    part = capacity // n_rep
    rep_index = lax.axis_index(REP)
    core_index = lax.axis_index(CORE)

    flat_ids = expert_ids.reshape(-1)
    onehot = (flat_ids[:, None] == jnp.arange(expert_count, dtype=jnp.int32)[None, :]).astype(
        jnp.int32
    )
    rank_counts = jnp.cumsum(onehot, axis=0) - onehot
    slot_index = jnp.sum(rank_counts * onehot, axis=1)
    source_rows = jnp.arange(tok_rows * top_count, dtype=jnp.int32) // top_count

    local_slot = slot_index - part * rep_index
    in_part = (local_slot >= 0) & (local_slot < part)
    send_slots = expert_count * part
    position = jnp.where(in_part, local_slot * expert_count + flat_ids, send_slots)
    table = jnp.zeros((send_slots,), jnp.int32).at[position].set(source_rows, mode="drop")
    outgoing = tokens[table].reshape(part, expert_count, 1, model_width)

    swap = [(0, 1), (1, 0)]
    other_gate, other_up, other_down = lax.ppermute((w_gate[0], w_up[0], w_down[0]), CORE, swap)
    gate_units = jnp.concatenate([w_gate[0], other_gate], axis=0)
    up_units = jnp.concatenate([w_up[0], other_up], axis=0)
    quarter = w_gate.shape[1]
    down_cols = jnp.concatenate([w_down[0], other_down], axis=1)
    col_count = down_cols.shape[1]
    down_split = down_cols.reshape(2, n_rep, quarter, col_count)
    own_half = lax.dynamic_index_in_dim(down_split, core_index, 0, keepdims=False)
    other_half = lax.dynamic_index_in_dim(down_split, 1 - core_index, 0, keepdims=False)
    down_units = jnp.stack([own_half, other_half], axis=1).reshape(n_rep, 2 * quarter, col_count)
    contract = (((1,), (1,)), ((), ()))

    lead = max(1, part - part // 2)
    spans = [(0, lead)] + ([(lead, part - lead)] if part > lead else [])
    chunks = []
    pick = jnp.zeros_like(slot_index)
    offset = 0
    plane = slot_index // part
    within = slot_index % part
    for first, size in spans:
        sending = outgoing[first:first + size].reshape(size, expert_count, model_width)
        arrived = lax.all_to_all(sending, GROUP, 1, 1, tiled=True)
        rows = lax.all_gather(arrived, REP, axis=0, tiled=False).reshape(-1, model_width)
        gate_proj = lax.dot_general(rows, gate_units, contract, preferred_element_type=jnp.float32)
        up_proj = lax.dot_general(rows, up_units, contract, preferred_element_type=jnp.float32)
        hidden = ((up_proj + 1.0) * gate_proj * jax.nn.sigmoid(1.702 * gate_proj)).astype(
            jnp.bfloat16
        )
        hidden_all = lax.all_gather(hidden, REP, axis=0, tiled=False)
        projected = jnp.einsum(
            "rnk,rkc->nc", hidden_all, down_units, preferred_element_type=jnp.float32
        )
        expert_out = projected.astype(jnp.bfloat16).reshape(n_rep, size, expert_count, col_count)
        back = lax.all_to_all(expert_out, GROUP, 2, 2, tiled=True)
        chunks.append(back.reshape(-1, col_count))
        here = offset + (plane * size + within - first) * expert_count + flat_ids
        in_span = (within >= first) & (within < first + size)
        pick = jnp.where(in_span, here, pick)
        offset += n_rep * size * expert_count

    returned = jnp.concatenate(chunks, axis=0)
    picked = returned[pick].astype(jnp.float32)
    levels = gate_levels.astype(jnp.float32)
    mixing = (levels / jnp.sum(levels, axis=1, keepdims=True)).reshape(-1, 1)
    combined = jnp.sum((mixing * picked).reshape(tok_rows, top_count, col_count), axis=1)
    combined = combined.reshape(tok_rows, 2, col_count // 2)
    ordered = jnp.where(core_index == 0, combined, combined[:, ::-1, :])
    return ordered.astype(jnp.bfloat16)


def solution(mesh):
    n_rep = mesh.shape[REP]
    n_exp = mesh.shape["exp"]
    split = Mesh(mesh.devices.reshape(n_rep, n_exp // 2, 2), (REP, GROUP, CORE))
    shards = (GROUP, CORE)
    return jax.shard_map(
        on_device,
        mesh=split,
        in_specs=(
            P(shards, None),
            P(shards, None),
            P(shards, None),
            P(shards, REP, None),
            P(shards, REP, None),
            P(shards, None, REP),
        ),
        out_specs=P(shards, None, REP),
        check_vma=False,
    )
```

```python
import jax
import jax.numpy as jnp
from jax import lax
from jax.sharding import Mesh
from jax.sharding import PartitionSpec as P

GROUP = ("gx", "gz")
CORE = "core"
REP = "rep"


def plane_all_to_all(value, axis):
    n_x = lax.axis_size(GROUP[0])
    n_z = lax.axis_size(GROUP[1])
    shape = value.shape
    split = value.reshape(*shape[:axis], n_x, n_z, *shape[axis + 1:])
    split = lax.all_to_all(split, GROUP[1], axis + 1, axis + 1, tiled=True)
    split = lax.all_to_all(split, GROUP[0], axis, axis, tiled=True)
    return split.reshape(shape)


def on_device(tokens, expert_ids, gate_levels, w_gate, w_up, w_down):
    tok_rows = tokens.shape[0]
    model_width = tokens.shape[1]
    top_count = expert_ids.shape[1]
    n_rep = lax.axis_size(REP)
    expert_count = lax.axis_size(GROUP[0]) * lax.axis_size(GROUP[1])
    capacity = min(
        tok_rows, max(4, (tok_rows * top_count * 3 // (2 * expert_count) + 3) // 4 * 4)
    )
    part = capacity // n_rep
    rep_index = lax.axis_index(REP)
    core_index = lax.axis_index(CORE)

    flat_ids = expert_ids.reshape(-1)
    onehot = (flat_ids[:, None] == jnp.arange(expert_count, dtype=jnp.int32)[None, :]).astype(
        jnp.int32
    )
    rank_counts = jnp.cumsum(onehot, axis=0) - onehot
    slot_index = jnp.sum(rank_counts * onehot, axis=1)
    source_rows = jnp.arange(tok_rows * top_count, dtype=jnp.int32) // top_count

    local_slot = slot_index - part * rep_index
    in_part = (local_slot >= 0) & (local_slot < part)
    send_slots = expert_count * part
    position = jnp.where(in_part, local_slot * expert_count + flat_ids, send_slots)
    table = jnp.zeros((send_slots,), jnp.int32).at[position].set(source_rows, mode="drop")
    outgoing = tokens[table].reshape(part, expert_count, 1, model_width)

    swap = [(0, 1), (1, 0)]
    other_gate, other_up, other_down = lax.ppermute((w_gate[0], w_up[0], w_down[0]), CORE, swap)
    gate_units = jnp.concatenate([w_gate[0], other_gate], axis=0)
    up_units = jnp.concatenate([w_up[0], other_up], axis=0)
    quarter = w_gate.shape[1]
    down_cols = jnp.concatenate([w_down[0], other_down], axis=1)
    col_count = down_cols.shape[1]
    down_split = down_cols.reshape(2, n_rep, quarter, col_count)
    own_half = lax.dynamic_index_in_dim(down_split, core_index, 0, keepdims=False)
    other_half = lax.dynamic_index_in_dim(down_split, 1 - core_index, 0, keepdims=False)
    down_units = jnp.stack([own_half, other_half], axis=1).reshape(n_rep, 2 * quarter, col_count)
    contract = (((1,), (1,)), ((), ()))

    lead = max(1, part - part // 2)
    spans = [(0, lead)] + ([(lead, part - lead)] if part > lead else [])
    chunks = []
    pick = jnp.zeros_like(slot_index)
    offset = 0
    plane = slot_index // part
    within = slot_index % part
    for first, size in spans:
        sending = outgoing[first:first + size].reshape(size, expert_count, model_width)
        arrived = plane_all_to_all(sending, 1)
        rows = lax.all_gather(arrived, REP, axis=0, tiled=False).reshape(-1, model_width)
        gate_proj = lax.dot_general(rows, gate_units, contract, preferred_element_type=jnp.float32)
        up_proj = lax.dot_general(rows, up_units, contract, preferred_element_type=jnp.float32)
        hidden = ((up_proj + 1.0) * gate_proj * jax.nn.sigmoid(1.702 * gate_proj)).astype(
            jnp.bfloat16
        )
        hidden_all = lax.all_gather(hidden, REP, axis=0, tiled=False)
        projected = jnp.einsum(
            "rnk,rkc->nc", hidden_all, down_units, preferred_element_type=jnp.float32
        )
        expert_out = projected.astype(jnp.bfloat16).reshape(n_rep, size, expert_count, col_count)
        back = plane_all_to_all(expert_out, 2)
        chunks.append(back.reshape(-1, col_count))
        here = offset + (plane * size + within - first) * expert_count + flat_ids
        in_span = (within >= first) & (within < first + size)
        pick = jnp.where(in_span, here, pick)
        offset += n_rep * size * expert_count

    returned = jnp.concatenate(chunks, axis=0)
    picked = returned[pick].astype(jnp.float32)
    levels = gate_levels.astype(jnp.float32)
    mixing = (levels / jnp.sum(levels, axis=1, keepdims=True)).reshape(-1, 1)
    combined = jnp.sum((mixing * picked).reshape(tok_rows, top_count, col_count), axis=1)
    combined = combined.reshape(tok_rows, 2, col_count // 2)
    ordered = jnp.where(core_index == 0, combined, combined[:, ::-1, :])
    return ordered.astype(jnp.bfloat16)


def solution(mesh):
    n_rep = mesh.shape[REP]
    n_exp = mesh.shape["exp"]
    n_z = len({device.coords[2] for device in mesh.devices.reshape(-1)})
    grid = mesh.devices.reshape(n_rep, n_exp // (2 * n_z), n_z, 2)
    split = Mesh(grid, (REP, *GROUP, CORE))
    shards = (*GROUP, CORE)
    return jax.shard_map(
        on_device,
        mesh=split,
        in_specs=(
            P(shards, None),
            P(shards, None),
            P(shards, None),
            P(shards, REP, None),
            P(shards, REP, None),
            P(shards, None, REP),
        ),
        out_specs=P(shards, None, REP),
        check_vma=False,
    )
```

```python
import jax
import jax.numpy as jnp
from jax import lax
from jax.sharding import Mesh
from jax.sharding import PartitionSpec as P

GROUP = "grp"
CORE = "core"
REP = "rep"


def on_device(tokens, expert_ids, gate_levels, w_gate, w_up, w_down):
    tok_rows = tokens.shape[0]
    model_width = tokens.shape[1]
    top_count = expert_ids.shape[1]
    n_rep = lax.axis_size(REP)
    expert_count = lax.axis_size(GROUP)
    capacity = min(
        tok_rows, max(4, (tok_rows * top_count * 3 // (2 * expert_count) + 3) // 4 * 4)
    )
    part = capacity // n_rep
    rep_index = lax.axis_index(REP)
    core_index = lax.axis_index(CORE)

    flat_ids = expert_ids.reshape(-1)
    onehot = (flat_ids[:, None] == jnp.arange(expert_count, dtype=jnp.int32)[None, :]).astype(
        jnp.int32
    )
    rank_counts = jnp.cumsum(onehot, axis=0) - onehot
    slot_index = jnp.sum(rank_counts * onehot, axis=1)
    source_rows = jnp.arange(tok_rows * top_count, dtype=jnp.int32) // top_count

    local_slot = slot_index - part * rep_index
    in_part = (local_slot >= 0) & (local_slot < part)
    send_slots = expert_count * part
    position = jnp.where(in_part, local_slot * expert_count + flat_ids, send_slots)
    table = jnp.zeros((send_slots,), jnp.int32).at[position].set(source_rows, mode="drop")
    outgoing = tokens[table].reshape(part, expert_count, 1, model_width)

    swap = [(0, 1), (1, 0)]
    other_gate, other_up, other_down = lax.ppermute((w_gate[0], w_up[0], w_down[0]), CORE, swap)
    gate_units = jnp.concatenate([w_gate[0], other_gate], axis=0)
    up_units = jnp.concatenate([w_up[0], other_up], axis=0)
    quarter = w_gate.shape[1]
    down_cols = jnp.concatenate([w_down[0], other_down], axis=1)
    col_count = down_cols.shape[1]
    down_split = down_cols.reshape(2, n_rep, quarter, col_count)
    own_half = lax.dynamic_index_in_dim(down_split, core_index, 0, keepdims=False)
    other_half = lax.dynamic_index_in_dim(down_split, 1 - core_index, 0, keepdims=False)
    down_units = jnp.stack([own_half, other_half], axis=1).reshape(n_rep, 2 * quarter, col_count)
    contract = (((1,), (1,)), ((), ()))

    lead = max(1, part - part // 2)
    spans = [(0, lead)] + ([(lead, part - lead)] if part > lead else [])
    chunks = []
    pick = jnp.zeros_like(slot_index)
    offset = 0
    plane = slot_index // part
    within = slot_index % part
    for first, size in spans:
        sending = outgoing[first:first + size].reshape(size, expert_count, model_width)
        arrived = lax.all_to_all(sending, GROUP, 1, 1, tiled=True)
        rows = lax.all_gather(arrived, REP, axis=0, tiled=False).reshape(-1, model_width)
        gate_proj = lax.dot_general(rows, gate_units, contract, preferred_element_type=jnp.float32)
        up_proj = lax.dot_general(rows, up_units, contract, preferred_element_type=jnp.float32)
        hidden = ((up_proj + 1.0) * gate_proj * jax.nn.sigmoid(1.702 * gate_proj)).astype(
            jnp.bfloat16
        )
        copies = jnp.broadcast_to(hidden[None], (n_rep, *hidden.shape))
        hidden_all = lax.all_to_all(copies, REP, 0, 0, tiled=True)
        projected = jnp.einsum(
            "rnk,rkc->nc", hidden_all, down_units, preferred_element_type=jnp.float32
        )
        expert_out = projected.astype(jnp.bfloat16).reshape(n_rep, size, expert_count, col_count)
        back = lax.all_to_all(expert_out, GROUP, 2, 2, tiled=True)
        chunks.append(back.reshape(-1, col_count))
        here = offset + (plane * size + within - first) * expert_count + flat_ids
        in_span = (within >= first) & (within < first + size)
        pick = jnp.where(in_span, here, pick)
        offset += n_rep * size * expert_count

    returned = jnp.concatenate(chunks, axis=0)
    picked = returned[pick].astype(jnp.float32)
    levels = gate_levels.astype(jnp.float32)
    mixing = (levels / jnp.sum(levels, axis=1, keepdims=True)).reshape(-1, 1)
    combined = jnp.sum((mixing * picked).reshape(tok_rows, top_count, col_count), axis=1)
    combined = combined.reshape(tok_rows, 2, col_count // 2)
    ordered = jnp.where(core_index == 0, combined, combined[:, ::-1, :])
    return ordered.astype(jnp.bfloat16)


def solution(mesh):
    n_rep = mesh.shape[REP]
    n_exp = mesh.shape["exp"]
    split = Mesh(mesh.devices.reshape(n_rep, n_exp // 2, 2), (REP, GROUP, CORE))
    shards = (GROUP, CORE)
    return jax.shard_map(
        on_device,
        mesh=split,
        in_specs=(
            P(shards, None),
            P(shards, None),
            P(shards, None),
            P(shards, REP, None),
            P(shards, REP, None),
            P(shards, None, REP),
        ),
        out_specs=P(shards, None, REP),
        check_vma=False,
    )
```

```python
import jax
import jax.numpy as jnp
from jax import lax
from jax.sharding import Mesh
from jax.sharding import PartitionSpec as P

GROUP = "grp"
CORE = "core"
REP = "rep"


def rep_gather(value, n_rep):
    copies = jnp.broadcast_to(value[None], (n_rep, *value.shape))
    return lax.all_to_all(copies, REP, 0, 0, tiled=True)


def on_device(tokens, expert_ids, gate_levels, w_gate, w_up, w_down):
    tok_rows = tokens.shape[0]
    model_width = tokens.shape[1]
    top_count = expert_ids.shape[1]
    n_rep = lax.axis_size(REP)
    expert_count = lax.axis_size(GROUP)
    capacity = min(
        tok_rows, max(4, (tok_rows * top_count * 3 // (2 * expert_count) + 3) // 4 * 4)
    )
    part = capacity // n_rep
    rep_index = lax.axis_index(REP)
    core_index = lax.axis_index(CORE)

    flat_ids = expert_ids.reshape(-1)
    onehot = (flat_ids[:, None] == jnp.arange(expert_count, dtype=jnp.int32)[None, :]).astype(
        jnp.int32
    )
    rank_counts = jnp.cumsum(onehot, axis=0) - onehot
    slot_index = jnp.sum(rank_counts * onehot, axis=1)
    source_rows = jnp.arange(tok_rows * top_count, dtype=jnp.int32) // top_count

    local_slot = slot_index - part * rep_index
    in_part = (local_slot >= 0) & (local_slot < part)
    send_slots = expert_count * part
    position = jnp.where(in_part, local_slot * expert_count + flat_ids, send_slots)
    table = jnp.zeros((send_slots,), jnp.int32).at[position].set(source_rows, mode="drop")
    outgoing = tokens[table].reshape(part, expert_count, 1, model_width)

    swap = [(0, 1), (1, 0)]
    other_gate, other_up, other_down = lax.ppermute((w_gate[0], w_up[0], w_down[0]), CORE, swap)
    gate_units = jnp.concatenate([w_gate[0], other_gate], axis=0)
    up_units = jnp.concatenate([w_up[0], other_up], axis=0)
    quarter = w_gate.shape[1]
    down_cols = jnp.concatenate([w_down[0], other_down], axis=1)
    col_count = down_cols.shape[1]
    down_split = down_cols.reshape(2, n_rep, quarter, col_count)
    own_half = lax.dynamic_index_in_dim(down_split, core_index, 0, keepdims=False)
    other_half = lax.dynamic_index_in_dim(down_split, 1 - core_index, 0, keepdims=False)
    down_units = jnp.stack([own_half, other_half], axis=1).reshape(n_rep, 2 * quarter, col_count)
    contract = (((1,), (1,)), ((), ()))

    chunks = []
    for chunk in range(part):
        arrived = lax.all_to_all(outgoing[chunk], GROUP, 0, 0, tiled=True)
        rows = rep_gather(arrived, n_rep).reshape(-1, model_width)
        gate_proj = lax.dot_general(rows, gate_units, contract, preferred_element_type=jnp.float32)
        up_proj = lax.dot_general(rows, up_units, contract, preferred_element_type=jnp.float32)
        hidden = ((up_proj + 1.0) * gate_proj * jax.nn.sigmoid(1.702 * gate_proj)).astype(
            jnp.bfloat16
        )
        hidden_all = rep_gather(hidden, n_rep)
        projected = jnp.einsum(
            "rnk,rkc->nc", hidden_all, down_units, preferred_element_type=jnp.float32
        )
        expert_out = projected.astype(jnp.bfloat16).reshape(n_rep, expert_count, col_count)
        chunks.append(lax.all_to_all(expert_out, GROUP, 1, 1, tiled=True))

    returned = jnp.stack(chunks, axis=0).reshape(-1, col_count)
    pick = ((slot_index % part) * n_rep + slot_index // part) * expert_count + flat_ids
    picked = returned[pick].astype(jnp.float32)
    levels = gate_levels.astype(jnp.float32)
    mixing = (levels / jnp.sum(levels, axis=1, keepdims=True)).reshape(-1, 1)
    combined = jnp.sum((mixing * picked).reshape(tok_rows, top_count, col_count), axis=1)
    combined = combined.reshape(tok_rows, 2, col_count // 2)
    ordered = jnp.where(core_index == 0, combined, combined[:, ::-1, :])
    return ordered.astype(jnp.bfloat16)


def solution(mesh):
    n_rep = mesh.shape[REP]
    n_exp = mesh.shape["exp"]
    split = Mesh(mesh.devices.reshape(n_rep, n_exp // 2, 2), (REP, GROUP, CORE))
    shards = (GROUP, CORE)
    return jax.shard_map(
        on_device,
        mesh=split,
        in_specs=(
            P(shards, None),
            P(shards, None),
            P(shards, None),
            P(shards, REP, None),
            P(shards, REP, None),
            P(shards, None, REP),
        ),
        out_specs=P(shards, None, REP),
        check_vma=False,
    )
```

```python
import jax
import jax.numpy as jnp
from jax import lax
from jax.sharding import Mesh
from jax.sharding import PartitionSpec as P

GROUP = "grp"
CORE = "core"
REP = "rep"


def on_device(tokens, expert_ids, gate_levels, w_gate, w_up, w_down):
    tok_rows = tokens.shape[0]
    model_width = tokens.shape[1]
    top_count = expert_ids.shape[1]
    n_rep = lax.axis_size(REP)
    expert_count = lax.axis_size(GROUP)
    capacity = min(
        tok_rows, max(4, (tok_rows * top_count * 3 // (2 * expert_count) + 3) // 4 * 4)
    )
    part = capacity // n_rep
    rep_index = lax.axis_index(REP)
    core_index = lax.axis_index(CORE)

    flat_ids = expert_ids.reshape(-1)
    onehot = (flat_ids[:, None] == jnp.arange(expert_count, dtype=jnp.int32)[None, :]).astype(
        jnp.int32
    )
    rank_counts = jnp.cumsum(onehot, axis=0) - onehot
    slot_index = jnp.sum(rank_counts * onehot, axis=1)

    local_slot = slot_index - part * rep_index
    in_part = (local_slot >= 0) & (local_slot < part)
    send_slots = expert_count * part
    position = jnp.where(in_part, local_slot * expert_count + flat_ids, send_slots)
    hits = position.reshape(tok_rows, top_count)[None, :, :] == jnp.arange(
        send_slots, dtype=jnp.int32
    )[:, None, None]
    select = jnp.any(hits, axis=2).astype(tokens.dtype)
    outgoing = jnp.dot(select, tokens, preferred_element_type=jnp.float32).astype(tokens.dtype)
    outgoing = outgoing.reshape(part, expert_count, 1, model_width)

    swap = [(0, 1), (1, 0)]
    other_gate, other_up, other_down = lax.ppermute((w_gate[0], w_up[0], w_down[0]), CORE, swap)
    gate_units = jnp.concatenate([w_gate[0], other_gate], axis=0)
    up_units = jnp.concatenate([w_up[0], other_up], axis=0)
    quarter = w_gate.shape[1]
    down_cols = jnp.concatenate([w_down[0], other_down], axis=1)
    col_count = down_cols.shape[1]
    down_split = down_cols.reshape(2, n_rep, quarter, col_count)
    own_half = lax.dynamic_index_in_dim(down_split, core_index, 0, keepdims=False)
    other_half = lax.dynamic_index_in_dim(down_split, 1 - core_index, 0, keepdims=False)
    down_units = jnp.stack([own_half, other_half], axis=1).reshape(n_rep, 2 * quarter, col_count)
    contract = (((1,), (1,)), ((), ()))

    chunks = []
    for chunk in range(part):
        arrived = lax.all_to_all(outgoing[chunk], GROUP, 0, 0, tiled=True)
        rows = lax.all_gather(arrived, REP, axis=0, tiled=False).reshape(-1, model_width)
        gate_proj = lax.dot_general(rows, gate_units, contract, preferred_element_type=jnp.float32)
        up_proj = lax.dot_general(rows, up_units, contract, preferred_element_type=jnp.float32)
        hidden = ((up_proj + 1.0) * gate_proj * jax.nn.sigmoid(1.702 * gate_proj)).astype(
            jnp.bfloat16
        )
        hidden_all = lax.all_gather(hidden, REP, axis=0, tiled=False)
        projected = jnp.einsum(
            "rnk,rkc->nc", hidden_all, down_units, preferred_element_type=jnp.float32
        )
        expert_out = projected.astype(jnp.bfloat16).reshape(n_rep, expert_count, col_count)
        chunks.append(lax.all_to_all(expert_out, GROUP, 1, 1, tiled=True))

    returned = jnp.stack(chunks, axis=0).reshape(-1, col_count)
    pick = ((slot_index % part) * n_rep + slot_index // part) * expert_count + flat_ids
    picked = returned[pick].astype(jnp.float32)
    levels = gate_levels.astype(jnp.float32)
    mixing = (levels / jnp.sum(levels, axis=1, keepdims=True)).reshape(-1, 1)
    combined = jnp.sum((mixing * picked).reshape(tok_rows, top_count, col_count), axis=1)
    combined = combined.reshape(tok_rows, 2, col_count // 2)
    ordered = jnp.where(core_index == 0, combined, combined[:, ::-1, :])
    return ordered.astype(jnp.bfloat16)


def solution(mesh):
    n_rep = mesh.shape[REP]
    n_exp = mesh.shape["exp"]
    split = Mesh(mesh.devices.reshape(n_rep, n_exp // 2, 2), (REP, GROUP, CORE))
    shards = (GROUP, CORE)
    return jax.shard_map(
        on_device,
        mesh=split,
        in_specs=(
            P(shards, None),
            P(shards, None),
            P(shards, None),
            P(shards, REP, None),
            P(shards, REP, None),
            P(shards, None, REP),
        ),
        out_specs=P(shards, None, REP),
        check_vma=False,
    )
```
